128 devices in a mesh: dp: 32 (over z_hi, x, y), mp: 4 (over z_lo, core).
Axes of the slice: x: 4, y: 4, z: 4 (z_hi: 2, z_lo: 2; z = z_hi * 2 + z_lo), core: 2. Of those that a mesh axis runs over, the one named last changes fastest.
Arguments:
- sample_grad: bfloat16 [4608, 8192], P('dp', 'mp'), may hold values from -3 to 3
- advantage: int32 [4608], P('dp'), may hold values from 1024 to 8191
- route_rows: int32 [32, 144], P('dp'), may hold values from 0 to 143, each once within a row
- route_count: int32 [32, 32], P('dp'), may hold values from 1 to 4, 80 in all within a row
- gate_pre: bfloat16 [4096, 16384], P('mp', 'dp'), may hold values from -5 to 5
- up_pre: bfloat16 [4096, 16384], P('mp', 'dp'), may hold values from -5 to 5
- down_weight: bfloat16 [16384, 8192], P('dp', 'mp'), may hold values from -0.046875 to 0.046875
Outputs:
- grad_down: float32 [16384, 8192], P('dp', 'mp')
- grad_gate: bfloat16 [4096, 16384], P('mp', 'dp')
- grad_up: bfloat16 [4096, 16384], P('mp', 'dp')
The draws below stay inside these ranges and needn't reach their ends.
Inputs may be any that keep to these rules, and one draw needn't show every extreme that they name: Each row of route_rows is a permutation of the sampler's 144 row numbers. `route_count`: each sampler sends every learner at least one row and 80 rows in all; in each sampler's row some learner receives exactly 4.
All inputs are finite; a program needn't handle non-finite values.
Results may differ from the reference program's by a relative error of at most 0.005.
Values may be sent and summed in bfloat16 or wider, within the bound.
No kernel may reach another device: no remote copies, remote signals or barrier semaphores. Data moves between devices by JAX's collectives and lax.ppermute only.
A program may use at most 128 MiB of HBM per device.

```python
import math
import jax
import jax.numpy as jnp
import numpy as np
from jax import lax

D = 8192
FF = 16384
SLOTS = 128
S_DEV = 144
T_TOTAL = 4096
S_TOTAL = 4608
N_DP = 32


def with_ends(result, stream_key, least, high):
    spot = [jax.random.randint(jax.random.fold_in(stream_key, axis), (), 0, length) for axis, length in enumerate(result.shape)]
    widest = result.shape.index(max(result.shape))
    beside = spot[:widest] + [(spot[widest] + 1) % result.shape[widest]] + spot[widest + 1:]
    return result.at[tuple(spot)].set(least).at[tuple(beside)].set(high)


def block_levels(rng, extent, cuts, least, largest):
    def one(position, blocks):
        steps = jax.random.uniform(jax.random.fold_in(jax.random.fold_in(rng, 6), position), (blocks,), jnp.float32, least / len(cuts), largest / len(cuts))
        return jnp.repeat(jnp.exp(steps), extent[position] // blocks).reshape((-1,) + (1,) * (len(extent) - position - 1))

    gain = one(*cuts[0])
    for cut in cuts[1:]:
        gain = gain * one(*cut)
    return gain


def profile(amount, total, limit, skew):
    portions = [(1 << 20) // math.isqrt(standing ** skew) + 1 for standing in range(2, amount + 1)]
    surplus, given = total - limit - (amount - 1), [1] * (amount - 1)
    while surplus > 0:
        movable = [i for i in range(amount - 1) if given[i] < limit]
        pool, budget = sum([portions[i] for i in movable]), surplus
        for i in movable:
            addition = min(limit - given[i], max(1, budget * portions[i] // pool), surplus)
            given[i] = given[i] + addition
            surplus = surplus - addition
    return np.array([limit] + given)


def uneven(own_key, count, total, reach, lean):
    if count == 2:
        one = jax.random.randint(own_key, (), max(1, total - reach), min(reach, total - 1) + 1)
        return jnp.stack([one, total - one])
    sizes = jnp.asarray(profile(count, total, reach, lean), jnp.int32)
    couples = (count - 1) // 2
    donor, taker = sizes[1:1 + 2 * couples:2], sizes[2:2 + 2 * couples:2]
    slack = jnp.minimum(donor - 1, reach - taker)
    moved = jax.random.randint(jax.random.fold_in(own_key, 1), (couples,), 0, 1 << 20) % (slack + 1)
    sizes = sizes.at[1:1 + 2 * couples:2].set(donor - moved).at[2:2 + 2 * couples:2].set(taker + moved)
    return sizes[jax.random.permutation(jax.random.fold_in(own_key, 2), count)]


def gaussian(own_key, extent, deviation, reach, pieces=(), held_as=jnp.bfloat16):
    level = block_levels(own_key, extent, pieces, -0.22, 0.18) if pieces else 1.0
    drawn = jax.random.normal(own_key, extent, jnp.float32) * deviation * level
    return jnp.minimum(jnp.maximum(drawn, -reach), reach).astype(held_as)


def setup_inputs(seed: int = 0) -> dict:
    streams_of = jax.random.split(jax.random.key(seed), 8)
    return {
        "sample_grad": gaussian(streams_of[0], (S_TOTAL, D), 0.5, 3.0, ((0, 32), (1, 4))),
        "advantage": with_ends(jax.random.randint(streams_of[1], (S_TOTAL,), 1024, 8192), jax.random.fold_in(streams_of[1], 1), 1024, 8191).astype(jnp.int32),
        "route_rows": jax.vmap(lambda own: jax.random.permutation(own, S_DEV))(jax.random.split(streams_of[2], N_DP)).reshape((N_DP, S_DEV)).astype(jnp.int32),
        "route_count": jax.vmap(lambda own: uneven(own, N_DP, SLOTS * 5 // 8, SLOTS // N_DP, 2))(jax.random.split(streams_of[3], N_DP)).reshape((N_DP, N_DP)).astype(jnp.int32),
        "gate_pre": gaussian(streams_of[4], (T_TOTAL, FF), 1.0, 5.0, ((0, 4), (1, 32))),
        "up_pre": gaussian(streams_of[5], (T_TOTAL, FF), 1.0, 5.0, ((0, 4), (1, 32))),
        "down_weight": gaussian(streams_of[6], (FF, D), FF ** -0.5, 0.046875, ((0, 32), (1, 4))),
    }


def silu_parts(gate_in):
    sigmoid_val = jax.nn.sigmoid(gate_in)
    return gate_in * sigmoid_val, sigmoid_val * (1.0 + gate_in * (1.0 - sigmoid_val))


def reference(sample_grad, advantage, route_rows, route_count, gate_pre, up_pre, down_weight):
    weights = advantage.astype(jnp.float32) * (1.0 / 4096.0)
    scaled = (sample_grad.astype(jnp.float32) * weights[:, None]).astype(jnp.bfloat16)
    capacity = SLOTS // N_DP
    route_table = route_rows[:, :SLOTS].reshape(N_DP, N_DP, capacity)
    offsets = (jnp.arange(N_DP, dtype=jnp.int32) * S_DEV)[:, None, None]
    source_rows = jnp.transpose(route_table + offsets, (1, 0, 2)).reshape(-1).astype(jnp.int32)
    live_mask = jnp.arange(capacity, dtype=jnp.int32)[None, None, :] < route_count[:, :, None]
    live_mask = jnp.transpose(live_mask, (1, 0, 2)).reshape(-1)
    slot_rows = jnp.where(live_mask[:, None], scaled[source_rows], jnp.zeros((), jnp.bfloat16))
    gate_in = gate_pre.astype(jnp.float32)
    up_in = up_pre.astype(jnp.float32)
    activated, slopes = silu_parts(gate_in)
    hidden = (activated * up_in).astype(jnp.bfloat16)
    grad_down = lax.dot_general(hidden, slot_rows, (((0,), (0,)), ((), ())), preferred_element_type=jnp.float32)
    hidden_grad = lax.dot_general(slot_rows, down_weight, (((1,), (1,)), ((), ())), preferred_element_type=jnp.float32)
    grad_gate = (hidden_grad * up_in * slopes).astype(jnp.bfloat16)
    grad_up = (hidden_grad * activated).astype(jnp.bfloat16)
    return grad_down, grad_gate, grad_up
```

```python
import jax
import jax.numpy as jnp
from jax import lax
from jax.sharding import PartitionSpec as P

SLOTS = 128
LIVE = SLOTS * 5 // 8


def silu_parts(gate_in):
    sigmoid_val = jax.nn.sigmoid(gate_in)
    return (gate_in * sigmoid_val, sigmoid_val * (1.0 + gate_in * (1.0 - sigmoid_val)))


def shards(sample_grad, advantage, route_rows, route_count, gate_pre, up_pre, down_weight):
    learners = lax.axis_size("dp")
    capacity = SLOTS // learners
    total_slots = learners * SLOTS

    counts = lax.all_gather(route_count.astype(jnp.float32), "dp", axis=0, tiled=True).astype(jnp.int32)
    own = lax.dynamic_index_in_dim(counts, lax.axis_index("dp"), axis=0, keepdims=False)

    gate_in = gate_pre.astype(jnp.float32)
    up_in = up_pre.astype(jnp.float32)
    activated, slopes = silu_parts(gate_in)
    hidden = (activated * up_in).astype(jnp.bfloat16)
    hidden, sample_grad = lax.optimization_barrier((hidden, sample_grad))
    n_mp = lax.axis_size("mp")
    pieces = [hidden] + [
        lax.ppermute(hidden, "mp", [(i, (i + s) % n_mp) for i in range(n_mp)]) for s in range(1, n_mp)
    ]
    stacked = jnp.concatenate(pieces, axis=0)

    own_end = jnp.cumsum(own)
    pos = jnp.arange(LIVE, dtype=jnp.int32)
    own_m = jnp.sum((own_end[None, :] <= pos[:, None]).astype(jnp.int32), axis=1)
    own_c = pos - (own_end[own_m] - own[own_m])
    picked = route_rows[0][own_m * capacity + own_c]
    weights = advantage.astype(jnp.float32) * (1.0 / 4096.0)
    scaled = (sample_grad[picked].astype(jnp.float32) * weights[picked][:, None]).astype(jnp.bfloat16)
    everything = lax.all_gather(scaled, "dp", axis=0, tiled=True)

    ends = jnp.cumsum(counts, axis=1)
    starts = ends - counts
    m_of = jnp.sum((ends[:, None, :] <= pos[None, :, None]).astype(jnp.int32), axis=2)
    c_of = pos[None, :] - jnp.take_along_axis(starts, m_of, axis=1)
    sender = jnp.arange(learners, dtype=jnp.int32)[:, None]
    slot_of = (m_of * SLOTS + sender * capacity + c_of).reshape(-1)

    rows_per = hidden.shape[0]
    shift = (lax.axis_index("mp") - slot_of // rows_per) % n_mp
    hidden_live = stacked[shift * rows_per + slot_of % rows_per]
    grad_down = lax.dot_general(
        hidden_live, everything, (((0,), (0,)), ((), ())), preferred_element_type=jnp.float32
    )
    partial_live = lax.dot_general(
        everything, down_weight, (((1,), (1,)), ((), ())), preferred_element_type=jnp.float32
    )

    t = jnp.arange(total_slots, dtype=jnp.int32)
    t_m = t // SLOTS
    t_k = (t % SLOTS) // capacity
    t_c = t % capacity
    live = t_c < counts[t_k, t_m]
    source = jnp.where(live, t_k * LIVE + starts[t_k, t_m] + t_c, 0)
    partial_value = jnp.where(live[:, None], partial_live[source], 0.0)
    hidden_grad = lax.psum_scatter(partial_value, "mp", scatter_dimension=0, tiled=True)
    grad_gate = (hidden_grad * up_in * slopes).astype(jnp.bfloat16)
    grad_up = (hidden_grad * activated).astype(jnp.bfloat16)
    return (grad_down, grad_gate, grad_up)


def solution(mesh):
    placed = (
        P("dp", "mp"),
        P("dp"),
        P("dp", None),
        P("dp", None),
        P("mp", "dp"),
        P("mp", "dp"),
        P("dp", "mp"),
    )
    return jax.shard_map(
        shards,
        mesh=mesh,
        in_specs=placed,
        out_specs=(P("dp", "mp"), P("mp", "dp"), P("mp", "dp")),
        check_vma=False,
    )
```

```python
import jax
import jax.numpy as jnp
from jax import lax
from jax.sharding import PartitionSpec as P

SLOTS = 128
LIVE = SLOTS * 5 // 8
INFO = 128


def silu_parts(gate_in):
    sigmoid_val = jax.nn.sigmoid(gate_in)
    return (gate_in * sigmoid_val, sigmoid_val * (1.0 + gate_in * (1.0 - sigmoid_val)))


def mp_gather(hidden):
    n_mp = lax.axis_size("mp")
    half = n_mp // 2
    me = lax.axis_index("mp")
    far = lax.ppermute(hidden, "mp", [(i, (i + half) % n_mp) for i in range(n_mp)])
    pair = jnp.stack([hidden, far])
    near = lax.ppermute(pair, "mp", [(i, i ^ 1) for i in range(n_mp)])
    held = jnp.concatenate([pair, near])
    block = jnp.arange(n_mp, dtype=jnp.int32)
    where = jnp.where(((block ^ me) % half) == 0, 0, 1) * 2 + jnp.where((block ^ me) >= half, 1, 0)
    return jnp.take(held, where, axis=0, mode="clip").reshape(n_mp * hidden.shape[0], hidden.shape[1])


def shards(sample_grad, advantage, route_rows, route_count, gate_pre, up_pre, down_weight):
    learners = lax.axis_size("dp")
    capacity = SLOTS // learners
    d_cols = sample_grad.shape[1]

    gate_in = gate_pre.astype(jnp.float32)
    up_in = up_pre.astype(jnp.float32)
    activated, slopes = silu_parts(gate_in)
    hidden = (activated * up_in).astype(jnp.bfloat16)
    hidden_all = mp_gather(hidden)

    own = route_count[0]
    own_end = jnp.cumsum(own)
    pos = jnp.arange(LIVE, dtype=jnp.int32)
    before = own_end[None, :] <= pos[:, None]
    own_m = jnp.sum(before.astype(jnp.int32), axis=1)
    own_c = pos - jnp.sum(jnp.where(before, own[None, :], 0), axis=1)
    picked = route_rows[0][own_m * capacity + own_c]
    weights = advantage.astype(jnp.float32) * (1.0 / 4096.0)
    scaled = (sample_grad[picked].astype(jnp.float32) * weights[picked][:, None]).astype(jnp.bfloat16)
    info = jnp.zeros((LIVE, INFO), jnp.bfloat16).at[0, :learners].set(own.astype(jnp.bfloat16))
    hidden_all, scaled = lax.optimization_barrier((hidden_all, scaled))
    sent = jnp.concatenate([scaled, info], axis=1)
    gathered = lax.all_gather(sent, "dp", axis=0, tiled=True)
    everything = gathered[:, :d_cols]
    counts = gathered.reshape(learners, LIVE, d_cols + INFO)[:, 0, d_cols:d_cols + learners]
    counts = counts.astype(jnp.int32)

    ends = jnp.cumsum(counts, axis=1)
    starts = ends - counts
    done = ends[:, None, :] <= pos[None, :, None]
    m_of = jnp.sum(done.astype(jnp.int32), axis=2)
    c_of = pos[None, :] - jnp.sum(jnp.where(done, counts[:, None, :], 0), axis=2)
    sender = jnp.arange(learners, dtype=jnp.int32)[:, None]
    slot_of = (m_of * SLOTS + sender * capacity + c_of).reshape(-1)

    hidden_live = hidden_all[slot_of]
    grad_down = lax.dot_general(
        hidden_live, everything, (((0,), (0,)), ((), ())), preferred_element_type=jnp.float32
    )
    partial_live = lax.dot_general(
        everything, down_weight, (((1,), (1,)), ((), ())), preferred_element_type=jnp.float32
    )

    lane = jnp.arange(capacity, dtype=jnp.int32)
    live = (lane[None, None, :] < counts.T[:, :, None]).reshape(-1)
    first = jnp.arange(learners, dtype=jnp.int32)[None, :] * LIVE + starts.T
    source = jnp.where(live, (first[:, :, None] + lane[None, None, :]).reshape(-1), 0)
    partial_value = jnp.where(live[:, None], partial_live[source], 0.0)
    hidden_grad = lax.psum_scatter(partial_value, "mp", scatter_dimension=0, tiled=True)
    grad_gate = (hidden_grad * up_in * slopes).astype(jnp.bfloat16)
    grad_up = (hidden_grad * activated).astype(jnp.bfloat16)
    return (grad_down, grad_gate, grad_up)


def solution(mesh):
    placed = (
        P("dp", "mp"),
        P("dp"),
        P("dp", None),
        P("dp", None),
        P("mp", "dp"),
        P("mp", "dp"),
        P("dp", "mp"),
    )
    return jax.shard_map(
        shards,
        mesh=mesh,
        in_specs=placed,
        out_specs=(P("dp", "mp"), P("mp", "dp"), P("mp", "dp")),
        check_vma=False,
    )
```

```python
import jax
import jax.numpy as jnp
from jax import lax
from jax.sharding import PartitionSpec as P

SLOTS = 128
LIVE = SLOTS * 5 // 8
INFO = 128


def silu_parts(gate_in):
    sigmoid_val = jax.nn.sigmoid(gate_in)
    return (gate_in * sigmoid_val, sigmoid_val * (1.0 + gate_in * (1.0 - sigmoid_val)))


def mp_gather(hidden):
    n_mp = lax.axis_size("mp")
    half = n_mp // 2
    me = lax.axis_index("mp")
    far = lax.ppermute(hidden, "mp", [(i, (i + half) % n_mp) for i in range(n_mp)])
    pair = jnp.stack([hidden, far])
    near = lax.ppermute(pair, "mp", [(i, i ^ 1) for i in range(n_mp)])
    held = jnp.concatenate([pair, near])
    block = jnp.arange(n_mp, dtype=jnp.int32)
    where = jnp.where(((block ^ me) % half) == 0, 0, 1) * 2 + jnp.where((block ^ me) >= half, 1, 0)
    return jnp.take(held, where, axis=0, mode="clip").reshape(n_mp * hidden.shape[0], hidden.shape[1])


def shards(sample_grad, advantage, route_rows, route_count, gate_pre, up_pre, down_weight):
    learners = lax.axis_size("dp")
    capacity = SLOTS // learners
    d_cols = sample_grad.shape[1]

    gate_in = gate_pre.astype(jnp.float32)
    up_in = up_pre.astype(jnp.float32)
    activated, slopes = silu_parts(gate_in)
    hidden = (activated * up_in).astype(jnp.bfloat16)

    own = route_count[0]
    own_end = jnp.cumsum(own)
    pos = jnp.arange(LIVE, dtype=jnp.int32)
    before = own_end[None, :] <= pos[:, None]
    own_m = jnp.sum(before.astype(jnp.int32), axis=1)
    own_c = pos - jnp.sum(jnp.where(before, own[None, :], 0), axis=1)
    picked = route_rows[0][own_m * capacity + own_c]
    weights = advantage.astype(jnp.float32) * (1.0 / 4096.0)
    scaled = (sample_grad[picked].astype(jnp.float32) * weights[picked][:, None]).astype(jnp.bfloat16)
    info = jnp.zeros((LIVE, INFO), jnp.bfloat16).at[0, :learners].set(own.astype(jnp.bfloat16))
    sent = jnp.concatenate([scaled, info], axis=1)
    sent, hidden = lax.optimization_barrier((sent, hidden))
    gathered = lax.all_gather(sent, "dp", axis=0, tiled=True)
    hidden_all = mp_gather(hidden)
    gathered, hidden_all = lax.optimization_barrier((gathered, hidden_all))
    everything = gathered[:, :d_cols]
    counts = gathered.reshape(learners, LIVE, d_cols + INFO)[:, 0, d_cols:d_cols + learners]
    counts = counts.astype(jnp.int32)

    ends = jnp.cumsum(counts, axis=1)
    starts = ends - counts
    done = ends[:, None, :] <= pos[None, :, None]
    m_of = jnp.sum(done.astype(jnp.int32), axis=2)
    c_of = pos[None, :] - jnp.sum(jnp.where(done, counts[:, None, :], 0), axis=2)
    sender = jnp.arange(learners, dtype=jnp.int32)[:, None]
    slot_of = (m_of * SLOTS + sender * capacity + c_of).reshape(-1)

    hidden_live = hidden_all[slot_of]
    grad_down = lax.dot_general(
        hidden_live, everything, (((0,), (0,)), ((), ())), preferred_element_type=jnp.float32
    )
    partial_live = lax.dot_general(
        everything, down_weight, (((1,), (1,)), ((), ())), preferred_element_type=jnp.float32
    )

    lane = jnp.arange(capacity, dtype=jnp.int32)
    live = (lane[None, None, :] < counts.T[:, :, None]).reshape(-1)
    first = jnp.arange(learners, dtype=jnp.int32)[None, :] * LIVE + starts.T
    source = jnp.where(live, (first[:, :, None] + lane[None, None, :]).reshape(-1), 0)

    me = lax.axis_index("mp")
    n_mp = lax.axis_size("mp")
    rows_per = hidden.shape[0]

    def partial_block(b):
        at = b * rows_per
        src = lax.dynamic_slice_in_dim(source, at, rows_per)
        keep = lax.dynamic_slice_in_dim(live, at, rows_per)
        return jnp.where(keep[:, None], partial_live[src], 0.0)

    to_core = jnp.stack([partial_block(me ^ 3), partial_block(me ^ 1)])
    from_core = lax.ppermute(to_core, "mp", [(i, i ^ 1) for i in range(n_mp)])
    to_chip = partial_block(me ^ 2) + from_core[0]
    from_chip = lax.ppermute(to_chip, "mp", [(i, i ^ 2) for i in range(n_mp)])
    hidden_grad = (partial_block(me) + from_core[1]) + from_chip
    grad_gate = (hidden_grad * up_in * slopes).astype(jnp.bfloat16)
    grad_up = (hidden_grad * activated).astype(jnp.bfloat16)
    return (grad_down, grad_gate, grad_up)


def solution(mesh):
    placed = (
        P("dp", "mp"),
        P("dp"),
        P("dp", None),
        P("dp", None),
        P("mp", "dp"),
        P("mp", "dp"),
        P("dp", "mp"),
    )
    return jax.shard_map(
        shards,
        mesh=mesh,
        in_specs=placed,
        out_specs=(P("dp", "mp"), P("mp", "dp"), P("mp", "dp")),
        check_vma=False,
    )
```

```python
import jax
import jax.numpy as jnp
from jax import lax
from jax.sharding import PartitionSpec as P

SLOTS = 128
LIVE = SLOTS * 5 // 8
INFO = 128


def silu_parts(gate_in):
    sigmoid_val = jax.nn.sigmoid(gate_in)
    return (gate_in * sigmoid_val, sigmoid_val * (1.0 + gate_in * (1.0 - sigmoid_val)))


def mp_gather(hidden):
    n_mp = lax.axis_size("mp")
    half = n_mp // 2
    me = lax.axis_index("mp")
    far = lax.ppermute(hidden, "mp", [(i, (i + half) % n_mp) for i in range(n_mp)])
    pair = jnp.stack([hidden, far])
    near = lax.ppermute(pair, "mp", [(i, i ^ 1) for i in range(n_mp)])
    held = jnp.concatenate([pair, near])
    block = jnp.arange(n_mp, dtype=jnp.int32)
    where = jnp.where(((block ^ me) % half) == 0, 0, 1) * 2 + jnp.where((block ^ me) >= half, 1, 0)
    return jnp.take(held, where, axis=0, mode="clip").reshape(n_mp * hidden.shape[0], hidden.shape[1])


def shards(sample_grad, advantage, route_rows, route_count, gate_pre, up_pre, down_weight):
    learners = lax.axis_size("dp")
    capacity = SLOTS // learners
    d_cols = sample_grad.shape[1]

    gate_in = gate_pre.astype(jnp.float32)
    up_in = up_pre.astype(jnp.float32)
    activated, slopes = silu_parts(gate_in)
    hidden = (activated * up_in).astype(jnp.bfloat16)

    own = route_count[0]
    own_end = jnp.cumsum(own)
    pos = jnp.arange(LIVE, dtype=jnp.int32)
    before = own_end[None, :] <= pos[:, None]
    own_m = jnp.sum(before.astype(jnp.int32), axis=1)
    own_c = pos - jnp.sum(jnp.where(before, own[None, :], 0), axis=1)
    picked = route_rows[0][own_m * capacity + own_c]
    weights = advantage.astype(jnp.float32) * (1.0 / 4096.0)
    scaled = (sample_grad[picked].astype(jnp.float32) * weights[picked][:, None]).astype(jnp.bfloat16)
    info = jnp.zeros((LIVE, INFO), jnp.bfloat16).at[0, :learners].set(own.astype(jnp.bfloat16))
    sent = jnp.concatenate([scaled, info], axis=1)
    sent, hidden = lax.optimization_barrier((sent, hidden))
    half = d_cols // 2
    left = lax.all_gather(sent[:, :half], "dp", axis=0, tiled=True)
    right = lax.all_gather(sent[:, half:], "dp", axis=0, tiled=True)
    hidden_all = mp_gather(hidden)
    left, right, hidden_all = lax.optimization_barrier((left, right, hidden_all))
    right_rows = right[:, :half]
    counts = right.reshape(learners, LIVE, half + INFO)[:, 0, half:half + learners]
    counts = counts.astype(jnp.int32)

    ends = jnp.cumsum(counts, axis=1)
    starts = ends - counts
    done = ends[:, None, :] <= pos[None, :, None]
    m_of = jnp.sum(done.astype(jnp.int32), axis=2)
    c_of = pos[None, :] - jnp.sum(jnp.where(done, counts[:, None, :], 0), axis=2)
    sender = jnp.arange(learners, dtype=jnp.int32)[:, None]
    slot_of = (m_of * SLOTS + sender * capacity + c_of).reshape(-1)

    hidden_live = hidden_all[slot_of]
    by_rows = (((0,), (0,)), ((), ()))
    grad_down = jnp.concatenate(
        [
            lax.dot_general(hidden_live, left, by_rows, preferred_element_type=jnp.float32),
            lax.dot_general(hidden_live, right_rows, by_rows, preferred_element_type=jnp.float32),
        ],
        axis=1,
    )
    by_cols = (((1,), (1,)), ((), ()))
    partial_live = lax.dot_general(
        left, down_weight[:, :half], by_cols, preferred_element_type=jnp.float32
    ) + lax.dot_general(right_rows, down_weight[:, half:], by_cols, preferred_element_type=jnp.float32)

    lane = jnp.arange(capacity, dtype=jnp.int32)
    live = (lane[None, None, :] < counts.T[:, :, None]).reshape(-1)
    first = jnp.arange(learners, dtype=jnp.int32)[None, :] * LIVE + starts.T
    source = jnp.where(live, (first[:, :, None] + lane[None, None, :]).reshape(-1), 0)

    me = lax.axis_index("mp")
    n_mp = lax.axis_size("mp")
    rows_per = hidden.shape[0]

    def partial_block(b):
        at = b * rows_per
        src = lax.dynamic_slice_in_dim(source, at, rows_per)
        keep = lax.dynamic_slice_in_dim(live, at, rows_per)
        return jnp.where(keep[:, None], partial_live[src], 0.0)

    to_core = jnp.stack([partial_block(me ^ 3), partial_block(me ^ 1)])
    from_core = lax.ppermute(to_core, "mp", [(i, i ^ 1) for i in range(n_mp)])
    to_chip = (partial_block(me ^ 2) + from_core[0]).astype(jnp.bfloat16)
    from_chip = lax.ppermute(to_chip, "mp", [(i, i ^ 2) for i in range(n_mp)])
    hidden_grad = (partial_block(me) + from_core[1]) + from_chip.astype(jnp.float32)
    grad_gate = (hidden_grad * up_in * slopes).astype(jnp.bfloat16)
    grad_up = (hidden_grad * activated).astype(jnp.bfloat16)
    return (grad_down, grad_gate, grad_up)


def solution(mesh):
    placed = (
        P("dp", "mp"),
        P("dp"),
        P("dp", None),
        P("dp", None),
        P("mp", "dp"),
        P("mp", "dp"),
        P("dp", "mp"),
    )
    return jax.shard_map(
        shards,
        mesh=mesh,
        in_specs=placed,
        out_specs=(P("dp", "mp"), P("mp", "dp"), P("mp", "dp")),
        check_vma=False,
    )
```

```python
import jax
import jax.numpy as jnp
from jax import lax
from jax.sharding import PartitionSpec as P

SLOTS = 128
LIVE = SLOTS * 5 // 8
INFO = 128


def silu_parts(gate_in):
    sigmoid_val = jax.nn.sigmoid(gate_in)
    return (gate_in * sigmoid_val, sigmoid_val * (1.0 + gate_in * (1.0 - sigmoid_val)))


def mp_gather(hidden):
    n_mp = lax.axis_size("mp")
    half = n_mp // 2
    me = lax.axis_index("mp")
    far = lax.ppermute(hidden, "mp", [(i, (i + half) % n_mp) for i in range(n_mp)])
    pair = jnp.stack([hidden, far])
    near = lax.ppermute(pair, "mp", [(i, i ^ 1) for i in range(n_mp)])
    held = jnp.concatenate([pair, near])
    block = jnp.arange(n_mp, dtype=jnp.int32)
    where = jnp.where(((block ^ me) % half) == 0, 0, 1) * 2 + jnp.where((block ^ me) >= half, 1, 0)
    return jnp.take(held, where, axis=0, mode="clip").reshape(n_mp * hidden.shape[0], hidden.shape[1])


def shards(sample_grad, advantage, route_rows, route_count, gate_pre, up_pre, down_weight):
    learners = lax.axis_size("dp")
    capacity = SLOTS // learners
    d_cols = sample_grad.shape[1]

    gate_in = gate_pre.astype(jnp.float32)
    up_in = up_pre.astype(jnp.float32)
    activated, slopes = silu_parts(gate_in)
    hidden = (activated * up_in).astype(jnp.bfloat16)

    own = route_count[0]
    own_end = jnp.cumsum(own)
    pos = jnp.arange(LIVE, dtype=jnp.int32)
    before = own_end[None, :] <= pos[:, None]
    own_m = jnp.sum(before.astype(jnp.int32), axis=1)
    own_c = pos - jnp.sum(jnp.where(before, own[None, :], 0), axis=1)
    picked = route_rows[0][own_m * capacity + own_c]
    weights = advantage.astype(jnp.float32) * (1.0 / 4096.0)
    scaled = (sample_grad[picked].astype(jnp.float32) * weights[picked][:, None]).astype(jnp.bfloat16)
    info = jnp.zeros((LIVE, INFO), jnp.bfloat16).at[0, :learners].set(own.astype(jnp.bfloat16))
    sent = jnp.concatenate([scaled, info], axis=1)
    sent, hidden = lax.optimization_barrier((sent, hidden))
    gathered = lax.all_gather(sent, "dp", axis=0, tiled=True)
    hidden_all = mp_gather(hidden)
    gathered, hidden_all = lax.optimization_barrier((gathered, hidden_all))
    everything = gathered[:, :d_cols]
    counts = gathered.reshape(learners, LIVE, d_cols + INFO)[:, 0, d_cols:d_cols + learners]
    counts = counts.astype(jnp.int32)

    ends = jnp.cumsum(counts, axis=1)
    starts = ends - counts
    done = ends[:, None, :] <= pos[None, :, None]
    m_of = jnp.sum(done.astype(jnp.int32), axis=2)
    c_of = pos[None, :] - jnp.sum(jnp.where(done, counts[:, None, :], 0), axis=2)
    sender = jnp.arange(learners, dtype=jnp.int32)[:, None]
    slot_of = (m_of * SLOTS + sender * capacity + c_of).reshape(-1)

    partial_live = lax.dot_general(
        everything, down_weight, (((1,), (1,)), ((), ())), preferred_element_type=jnp.float32
    )

    lane = jnp.arange(capacity, dtype=jnp.int32)
    live = (lane[None, None, :] < counts.T[:, :, None]).reshape(-1)
    first = jnp.arange(learners, dtype=jnp.int32)[None, :] * LIVE + starts.T
    source = jnp.where(live, (first[:, :, None] + lane[None, None, :]).reshape(-1), 0)

    me = lax.axis_index("mp")
    n_mp = lax.axis_size("mp")
    rows_per = hidden.shape[0]

    def partial_block(b):
        at = b * rows_per
        src = lax.dynamic_slice_in_dim(source, at, rows_per)
        keep = lax.dynamic_slice_in_dim(live, at, rows_per)
        return jnp.where(keep[:, None], partial_live[src], 0.0)

    to_core = jnp.stack([partial_block(me ^ 3), partial_block(me ^ 1)])
    from_core = lax.ppermute(to_core, "mp", [(i, i ^ 1) for i in range(n_mp)])
    to_chip = (partial_block(me ^ 2) + from_core[0]).astype(jnp.bfloat16)
    from_chip = lax.ppermute(to_chip, "mp", [(i, i ^ 2) for i in range(n_mp)])
    own_part = partial_block(me) + from_core[1]

    to_chip, hidden_all = lax.optimization_barrier((to_chip, hidden_all))
    hidden_live = hidden_all[slot_of]
    grad_down = lax.dot_general(
        hidden_live, everything, (((0,), (0,)), ((), ())), preferred_element_type=jnp.float32
    )
    hidden_grad = own_part + from_chip.astype(jnp.float32)
    grad_gate = (hidden_grad * up_in * slopes).astype(jnp.bfloat16)
    grad_up = (hidden_grad * activated).astype(jnp.bfloat16)
    return (grad_down, grad_gate, grad_up)


def solution(mesh):
    placed = (
        P("dp", "mp"),
        P("dp"),
        P("dp", None),
        P("dp", None),
        P("mp", "dp"),
        P("mp", "dp"),
        P("dp", "mp"),
    )
    return jax.shard_map(
        shards,
        mesh=mesh,
        in_specs=placed,
        out_specs=(P("dp", "mp"), P("mp", "dp"), P("mp", "dp")),
        check_vma=False,
    )
```

```python
import jax
import jax.numpy as jnp
from jax import lax
from jax.sharding import PartitionSpec as P

SLOTS = 128
LIVE = SLOTS * 5 // 8
INFO = 128


def silu_parts(gate_in):
    sigmoid_val = jax.nn.sigmoid(gate_in)
    return (gate_in * sigmoid_val, sigmoid_val * (1.0 + gate_in * (1.0 - sigmoid_val)))


def mp_gather(hidden):
    n_mp = lax.axis_size("mp")
    half = n_mp // 2
    me = lax.axis_index("mp")
    far = lax.ppermute(hidden, "mp", [(i, (i + half) % n_mp) for i in range(n_mp)])
    pair = jnp.stack([hidden, far])
    near = lax.ppermute(pair, "mp", [(i, i ^ 1) for i in range(n_mp)])
    held = jnp.concatenate([pair, near])
    block = jnp.arange(n_mp, dtype=jnp.int32)
    where = jnp.where(((block ^ me) % half) == 0, 0, 1) * 2 + jnp.where((block ^ me) >= half, 1, 0)
    return jnp.take(held, where, axis=0, mode="clip").reshape(n_mp * hidden.shape[0], hidden.shape[1])


def shards(sample_grad, advantage, route_rows, route_count, gate_pre, up_pre, down_weight):
    learners = lax.axis_size("dp")
    capacity = SLOTS // learners
    d_cols = sample_grad.shape[1]

    gate_in = gate_pre.astype(jnp.float32)
    up_in = up_pre.astype(jnp.float32)
    activated, slopes = silu_parts(gate_in)
    hidden = (activated * up_in).astype(jnp.bfloat16)

    own = route_count[0]
    own_end = jnp.cumsum(own)
    pos = jnp.arange(LIVE, dtype=jnp.int32)
    before = own_end[None, :] <= pos[:, None]
    own_m = jnp.sum(before.astype(jnp.int32), axis=1)
    own_c = pos - jnp.sum(jnp.where(before, own[None, :], 0), axis=1)
    picked = route_rows[0][own_m * capacity + own_c]
    weights = advantage.astype(jnp.float32) * (1.0 / 4096.0)
    scaled = (sample_grad[picked].astype(jnp.float32) * weights[picked][:, None]).astype(jnp.bfloat16)
    info = jnp.zeros((LIVE, INFO), jnp.bfloat16).at[0, :learners].set(own.astype(jnp.bfloat16))
    sent = jnp.concatenate([scaled, info], axis=1)
    sent, hidden = lax.optimization_barrier((sent, hidden))
    me_dp = lax.axis_index("dp")
    gathered = jnp.concatenate(
        [sent]
        + [lax.ppermute(sent, "dp", [(i, (i + s) % learners) for i in range(learners)]) for s in range(1, learners)],
        axis=0,
    )
    hidden_all = mp_gather(hidden)
    gathered, hidden_all = lax.optimization_barrier((gathered, hidden_all))
    everything = gathered[:, :d_cols]
    counts = gathered.reshape(learners, LIVE, d_cols + INFO)[:, 0, d_cols:d_cols + learners]
    counts = counts.astype(jnp.int32)
    block_sampler = (me_dp - jnp.arange(learners, dtype=jnp.int32)) % learners

    ends = jnp.cumsum(counts, axis=1)
    starts = ends - counts
    done = ends[:, None, :] <= pos[None, :, None]
    m_of = jnp.sum(done.astype(jnp.int32), axis=2)
    c_of = pos[None, :] - jnp.sum(jnp.where(done, counts[:, None, :], 0), axis=2)
    slot_of = (m_of * SLOTS + block_sampler[:, None] * capacity + c_of).reshape(-1)

    partial_live = lax.dot_general(
        everything, down_weight, (((1,), (1,)), ((), ())), preferred_element_type=jnp.float32
    )

    lane = jnp.arange(capacity, dtype=jnp.int32)
    by_sampler = jnp.roll(counts[::-1], me_dp - (learners - 1), axis=0)
    live = (lane[None, None, :] < by_sampler.T[:, :, None]).reshape(-1)
    sampler_start = jnp.cumsum(by_sampler, axis=1) - by_sampler
    first = block_sampler[None, :] * LIVE + sampler_start.T
    source = jnp.where(live, (first[:, :, None] + lane[None, None, :]).reshape(-1), 0)

    me = lax.axis_index("mp")
    n_mp = lax.axis_size("mp")
    rows_per = hidden.shape[0]

    def partial_block(b):
        at = b * rows_per
        src = lax.dynamic_slice_in_dim(source, at, rows_per)
        keep = lax.dynamic_slice_in_dim(live, at, rows_per)
        return jnp.where(keep[:, None], partial_live[src], 0.0)

    to_core = jnp.stack([partial_block(me ^ 3), partial_block(me ^ 1)])
    from_core = lax.ppermute(to_core, "mp", [(i, i ^ 1) for i in range(n_mp)])
    to_chip = (partial_block(me ^ 2) + from_core[0]).astype(jnp.bfloat16)
    from_chip = lax.ppermute(to_chip, "mp", [(i, i ^ 2) for i in range(n_mp)])
    own_part = partial_block(me) + from_core[1]

    to_chip, hidden_all = lax.optimization_barrier((to_chip, hidden_all))
    hidden_live = hidden_all[slot_of]
    grad_down = lax.dot_general(
        hidden_live, everything, (((0,), (0,)), ((), ())), preferred_element_type=jnp.float32
    )
    hidden_grad = own_part + from_chip.astype(jnp.float32)
    grad_gate = (hidden_grad * up_in * slopes).astype(jnp.bfloat16)
    grad_up = (hidden_grad * activated).astype(jnp.bfloat16)
    return (grad_down, grad_gate, grad_up)


def solution(mesh):
    placed = (
        P("dp", "mp"),
        P("dp"),
        P("dp", None),
        P("dp", None),
        P("mp", "dp"),
        P("mp", "dp"),
        P("dp", "mp"),
    )
    return jax.shard_map(
        shards,
        mesh=mesh,
        in_specs=placed,
        out_specs=(P("dp", "mp"), P("mp", "dp"), P("mp", "dp")),
        check_vma=False,
    )
```

```python
import jax
import jax.numpy as jnp
from jax import lax
from jax.sharding import PartitionSpec as P

SLOTS = 128
LIVE = SLOTS * 5 // 8
INFO = 128


def silu_parts(gate_in):
    sigmoid_val = jax.nn.sigmoid(gate_in)
    return (gate_in * sigmoid_val, sigmoid_val * (1.0 + gate_in * (1.0 - sigmoid_val)))


def mp_gather(hidden):
    n_mp = lax.axis_size("mp")
    half = n_mp // 2
    me = lax.axis_index("mp")
    far = lax.ppermute(hidden, "mp", [(i, (i + half) % n_mp) for i in range(n_mp)])
    pair = jnp.stack([hidden, far])
    near = lax.ppermute(pair, "mp", [(i, i ^ 1) for i in range(n_mp)])
    held = jnp.concatenate([pair, near])
    block = jnp.arange(n_mp, dtype=jnp.int32)
    where = jnp.where(((block ^ me) % half) == 0, 0, 1) * 2 + jnp.where((block ^ me) >= half, 1, 0)
    return jnp.take(held, where, axis=0, mode="clip").reshape(n_mp * hidden.shape[0], hidden.shape[1])


def shards(sample_grad, advantage, route_rows, route_count, gate_pre, up_pre, down_weight):
    learners = lax.axis_size("dp")
    capacity = SLOTS // learners
    d_cols = sample_grad.shape[1]


    own = route_count[0]
    own_end = jnp.cumsum(own)
    pos = jnp.arange(LIVE, dtype=jnp.int32)
    before = own_end[None, :] <= pos[:, None]
    own_m = jnp.sum(before.astype(jnp.int32), axis=1)
    own_c = pos - jnp.sum(jnp.where(before, own[None, :], 0), axis=1)
    picked = route_rows[0][own_m * capacity + own_c]
    weights = advantage.astype(jnp.float32) * (1.0 / 4096.0)
    scaled = (sample_grad[picked].astype(jnp.float32) * weights[picked][:, None]).astype(jnp.bfloat16)
    info = jnp.zeros((LIVE, INFO), jnp.bfloat16).at[0, :learners].set(own.astype(jnp.bfloat16))
    sent = jnp.concatenate([scaled, info], axis=1)
    sent, gate_late, up_late = lax.optimization_barrier((sent, gate_pre, up_pre))
    gate_in = gate_late.astype(jnp.float32)
    up_in = up_late.astype(jnp.float32)
    activated, slopes = silu_parts(gate_in)
    hidden = (activated * up_in).astype(jnp.bfloat16)
    gathered = lax.all_gather(sent, "dp", axis=0, tiled=True)
    hidden_all = mp_gather(hidden)
    gathered, hidden_all = lax.optimization_barrier((gathered, hidden_all))
    everything = gathered[:, :d_cols]
    counts = gathered.reshape(learners, LIVE, d_cols + INFO)[:, 0, d_cols:d_cols + learners]
    counts = counts.astype(jnp.int32)

    ends = jnp.cumsum(counts, axis=1)
    starts = ends - counts
    done = ends[:, None, :] <= pos[None, :, None]
    m_of = jnp.sum(done.astype(jnp.int32), axis=2)
    c_of = pos[None, :] - jnp.sum(jnp.where(done, counts[:, None, :], 0), axis=2)
    sender = jnp.arange(learners, dtype=jnp.int32)[:, None]
    slot_of = (m_of * SLOTS + sender * capacity + c_of).reshape(-1)

    partial_live = lax.dot_general(
        everything, down_weight, (((1,), (1,)), ((), ())), preferred_element_type=jnp.float32
    )

    lane = jnp.arange(capacity, dtype=jnp.int32)
    live = (lane[None, None, :] < counts.T[:, :, None]).reshape(-1)
    first = jnp.arange(learners, dtype=jnp.int32)[None, :] * LIVE + starts.T
    source = jnp.where(live, (first[:, :, None] + lane[None, None, :]).reshape(-1), 0)

    me = lax.axis_index("mp")
    n_mp = lax.axis_size("mp")
    rows_per = hidden.shape[0]

    def partial_block(partial, b):
        at = b * rows_per
        src = lax.dynamic_slice_in_dim(source, at, rows_per)
        keep = lax.dynamic_slice_in_dim(live, at, rows_per)
        return jnp.where(keep[:, None], partial[src], 0.0)

    pairs_core = [(i, i ^ 1) for i in range(n_mp)]
    from_core = lax.ppermute(partial_block(partial_live, me ^ 3), "mp", pairs_core)
    to_chip = (partial_block(partial_live, me ^ 2) + from_core).astype(jnp.bfloat16)
    to_chip, partial_late, hidden_all = lax.optimization_barrier((to_chip, partial_live, hidden_all))
    from_chip = lax.ppermute(to_chip, "mp", [(i, i ^ 2) for i in range(n_mp)])
    from_core_own = lax.ppermute(partial_block(partial_late, me ^ 1), "mp", pairs_core)
    own_part = partial_block(partial_late, me)
    hidden_live = hidden_all[slot_of]
    grad_down = lax.dot_general(
        hidden_live, everything, (((0,), (0,)), ((), ())), preferred_element_type=jnp.float32
    )
    hidden_grad = (own_part + from_core_own) + from_chip.astype(jnp.float32)
    grad_gate = (hidden_grad * up_in * slopes).astype(jnp.bfloat16)
    grad_up = (hidden_grad * activated).astype(jnp.bfloat16)
    return (grad_down, grad_gate, grad_up)


def solution(mesh):
    placed = (
        P("dp", "mp"),
        P("dp"),
        P("dp", None),
        P("dp", None),
        P("mp", "dp"),
        P("mp", "dp"),
        P("dp", "mp"),
    )
    return jax.shard_map(
        shards,
        mesh=mesh,
        in_specs=placed,
        out_specs=(P("dp", "mp"), P("mp", "dp"), P("mp", "dp")),
        check_vma=False,
    )
```

```python
import jax
import jax.numpy as jnp
from jax import lax
from jax.sharding import PartitionSpec as P

SLOTS = 128
LIVE = SLOTS * 5 // 8


def silu_parts(gate_in):
    sigmoid_val = jax.nn.sigmoid(gate_in)
    return (gate_in * sigmoid_val, sigmoid_val * (1.0 + gate_in * (1.0 - sigmoid_val)))


def mp_gather(hidden):
    n_mp = lax.axis_size("mp")
    half = n_mp // 2
    me = lax.axis_index("mp")
    far = lax.ppermute(hidden, "mp", [(i, (i + half) % n_mp) for i in range(n_mp)])
    pair = jnp.stack([hidden, far])
    near = lax.ppermute(pair, "mp", [(i, i ^ 1) for i in range(n_mp)])
    held = jnp.concatenate([pair, near])
    block = jnp.arange(n_mp, dtype=jnp.int32)
    where = jnp.where(((block ^ me) % half) == 0, 0, 1) * 2 + jnp.where((block ^ me) >= half, 1, 0)
    return jnp.take(held, where, axis=0, mode="clip").reshape(n_mp * hidden.shape[0], hidden.shape[1])


def dp_gather_small(block):
    n = lax.axis_size("dp")
    me = lax.axis_index("dp")
    held = block
    step = 1
    while step < n:
        theirs = lax.ppermute(held, "dp", [(i, i ^ step) for i in range(n)])
        low = (me & step) == 0
        held = jnp.where(low, jnp.concatenate([held, theirs]), jnp.concatenate([theirs, held]))
        step *= 2
    return held


def shards(sample_grad, advantage, route_rows, route_count, gate_pre, up_pre, down_weight):
    learners = lax.axis_size("dp")
    capacity = SLOTS // learners

    own = route_count[0]
    own_end = jnp.cumsum(own)
    pos = jnp.arange(LIVE, dtype=jnp.int32)
    before = own_end[None, :] <= pos[:, None]
    own_m = jnp.sum(before.astype(jnp.int32), axis=1)
    own_c = pos - jnp.sum(jnp.where(before, own[None, :], 0), axis=1)
    picked = route_rows[0][own_m * capacity + own_c]
    weights = advantage.astype(jnp.float32) * (1.0 / 4096.0)
    scaled = (sample_grad[picked].astype(jnp.float32) * weights[picked][:, None]).astype(jnp.bfloat16)
    sent, gate_late, up_late, own_late = lax.optimization_barrier((scaled, gate_pre, up_pre, route_count))
    gate_in = gate_late.astype(jnp.float32)
    up_in = up_late.astype(jnp.float32)
    activated, slopes = silu_parts(gate_in)
    hidden = (activated * up_in).astype(jnp.bfloat16)
    gathered = lax.all_gather(sent, "dp", axis=0, tiled=True)
    hidden_all = mp_gather(hidden)
    counts = dp_gather_small(own_late)

    everything = gathered

    ends = jnp.cumsum(counts, axis=1)
    starts = ends - counts
    done = ends[:, None, :] <= pos[None, :, None]
    m_of = jnp.sum(done.astype(jnp.int32), axis=2)
    c_of = pos[None, :] - jnp.sum(jnp.where(done, counts[:, None, :], 0), axis=2)
    sender = jnp.arange(learners, dtype=jnp.int32)[:, None]
    slot_of = (m_of * SLOTS + sender * capacity + c_of).reshape(-1)
    hidden_live = hidden_all[slot_of]
    everything, hidden_live = lax.optimization_barrier((everything, hidden_live))

    partial_live = lax.dot_general(
        everything, down_weight, (((1,), (1,)), ((), ())), preferred_element_type=jnp.float32
    )

    lane = jnp.arange(capacity, dtype=jnp.int32)
    live = (lane[None, None, :] < counts.T[:, :, None]).reshape(-1)
    first = jnp.arange(learners, dtype=jnp.int32)[None, :] * LIVE + starts.T
    source = jnp.where(live, (first[:, :, None] + lane[None, None, :]).reshape(-1), 0)

    me = lax.axis_index("mp")
    n_mp = lax.axis_size("mp")
    rows_per = hidden.shape[0]

    def partial_block(partial, b):
        at = b * rows_per
        src = lax.dynamic_slice_in_dim(source, at, rows_per)
        keep = lax.dynamic_slice_in_dim(live, at, rows_per)
        return jnp.where(keep[:, None], partial[src], 0.0)

    pairs_core = [(i, i ^ 1) for i in range(n_mp)]
    from_core = lax.ppermute(partial_block(partial_live, me ^ 3), "mp", pairs_core)
    to_chip = (partial_block(partial_live, me ^ 2) + from_core).astype(jnp.bfloat16)
    to_chip, partial_late = lax.optimization_barrier((to_chip, partial_live))
    from_chip = lax.ppermute(to_chip, "mp", [(i, i ^ 2) for i in range(n_mp)])
    from_core_own = lax.ppermute(partial_block(partial_late, me ^ 1), "mp", pairs_core)
    own_part = partial_block(partial_late, me)
    grad_down = lax.dot_general(
        hidden_live, everything, (((0,), (0,)), ((), ())), preferred_element_type=jnp.float32
    )
    hidden_grad = (own_part + from_core_own) + from_chip.astype(jnp.float32)
    grad_gate = (hidden_grad * up_in * slopes).astype(jnp.bfloat16)
    grad_up = (hidden_grad * activated).astype(jnp.bfloat16)
    return (grad_down, grad_gate, grad_up)


def solution(mesh):
    placed = (
        P("dp", "mp"),
        P("dp"),
        P("dp", None),
        P("dp", None),
        P("mp", "dp"),
        P("mp", "dp"),
        P("dp", "mp"),
    )
    return jax.shard_map(
        shards,
        mesh=mesh,
        in_specs=placed,
        out_specs=(P("dp", "mp"), P("mp", "dp"), P("mp", "dp")),
        check_vma=False,
    )
```

```python
import jax
import jax.numpy as jnp
from jax import lax
from jax.sharding import PartitionSpec as P

SLOTS = 128
LIVE = SLOTS * 5 // 8


def silu_parts(gate_in):
    sigmoid_val = jax.nn.sigmoid(gate_in)
    return (gate_in * sigmoid_val, sigmoid_val * (1.0 + gate_in * (1.0 - sigmoid_val)))


def mp_gather(hidden):
    n_mp = lax.axis_size("mp")
    half = n_mp // 2
    me = lax.axis_index("mp")
    far = lax.ppermute(hidden, "mp", [(i, (i + half) % n_mp) for i in range(n_mp)])
    pair = jnp.stack([hidden, far])
    near = lax.ppermute(pair, "mp", [(i, i ^ 1) for i in range(n_mp)])
    held = jnp.concatenate([pair, near])
    block = jnp.arange(n_mp, dtype=jnp.int32)
    where = jnp.where(((block ^ me) % half) == 0, 0, 1) * 2 + jnp.where((block ^ me) >= half, 1, 0)
    return jnp.take(held, where, axis=0, mode="clip").reshape(n_mp * hidden.shape[0], hidden.shape[1])


def dp_gather_small(block):
    n = lax.axis_size("dp")
    me = lax.axis_index("dp")
    held = block
    step = 1
    while step < n:
        theirs = lax.ppermute(held, "dp", [(i, i ^ step) for i in range(n)])
        low = (me & step) == 0
        held = jnp.where(low, jnp.concatenate([held, theirs]), jnp.concatenate([theirs, held]))
        step *= 2
    return held


def shards(sample_grad, advantage, route_rows, route_count, gate_pre, up_pre, down_weight):
    learners = lax.axis_size("dp")
    capacity = SLOTS // learners

    own = route_count[0]
    own_end = jnp.cumsum(own)
    pos = jnp.arange(LIVE, dtype=jnp.int32)
    before = own_end[None, :] <= pos[:, None]
    own_m = jnp.sum(before.astype(jnp.int32), axis=1)
    own_c = pos - jnp.sum(jnp.where(before, own[None, :], 0), axis=1)
    picked = route_rows[0][own_m * capacity + own_c]
    weights = advantage.astype(jnp.float32) * (1.0 / 4096.0)
    scaled = (sample_grad[picked].astype(jnp.float32) * weights[picked][:, None]).astype(jnp.bfloat16)
    sent, gate_late, up_late, own_late = lax.optimization_barrier((scaled, gate_pre, up_pre, route_count))
    gate_in = gate_late.astype(jnp.float32)
    up_in = up_late.astype(jnp.float32)
    activated, slopes = silu_parts(gate_in)
    hidden = (activated * up_in).astype(jnp.bfloat16)
    gathered = lax.all_gather(sent, "dp", axis=0, tiled=True)
    hidden_all = mp_gather(hidden)
    counts = dp_gather_small(own_late)

    everything = gathered

    ends = jnp.cumsum(counts, axis=1)
    starts = ends - counts
    done = ends[:, None, :] <= pos[None, :, None]
    m_of = jnp.sum(done.astype(jnp.int32), axis=2)
    c_of = pos[None, :] - jnp.sum(jnp.where(done, counts[:, None, :], 0), axis=2)
    sender = jnp.arange(learners, dtype=jnp.int32)[:, None]
    slot_of = (m_of * SLOTS + sender * capacity + c_of).reshape(-1)
    hidden_live = hidden_all[slot_of]
    everything, hidden_live = lax.optimization_barrier((everything, hidden_live))

    partial_live = lax.dot_general(
        everything, down_weight, (((1,), (1,)), ((), ())), preferred_element_type=jnp.float32
    )

    lane = jnp.arange(capacity, dtype=jnp.int32)
    live = (lane[None, None, :] < counts.T[:, :, None]).reshape(-1)
    first = jnp.arange(learners, dtype=jnp.int32)[None, :] * LIVE + starts.T
    source = jnp.where(live, (first[:, :, None] + lane[None, None, :]).reshape(-1), 0)

    me = lax.axis_index("mp")
    n_mp = lax.axis_size("mp")
    rows_per = hidden.shape[0]

    def partial_block(partial, b):
        return partial[lax.dynamic_slice_in_dim(source, b * rows_per, rows_per)]

    pairs_core = [(i, i ^ 1) for i in range(n_mp)]
    from_core = lax.ppermute(partial_block(partial_live, me ^ 3), "mp", pairs_core)
    to_chip = (partial_block(partial_live, me ^ 2) + from_core).astype(jnp.bfloat16)
    to_chip, partial_late = lax.optimization_barrier((to_chip, partial_live))
    from_chip = lax.ppermute(to_chip, "mp", [(i, i ^ 2) for i in range(n_mp)])
    from_core_own = lax.ppermute(partial_block(partial_late, me ^ 1), "mp", pairs_core)
    own_part = partial_block(partial_late, me)
    grad_down = lax.dot_general(
        hidden_live, everything, (((0,), (0,)), ((), ())), preferred_element_type=jnp.float32
    )
    hidden_grad = (own_part + from_core_own) + from_chip.astype(jnp.float32)
    hidden_grad = jnp.where(lax.dynamic_slice_in_dim(live, me * rows_per, rows_per)[:, None], hidden_grad, 0.0)
    grad_gate = (hidden_grad * up_in * slopes).astype(jnp.bfloat16)
    grad_up = (hidden_grad * activated).astype(jnp.bfloat16)
    return (grad_down, grad_gate, grad_up)


def solution(mesh):
    placed = (
        P("dp", "mp"),
        P("dp"),
        P("dp", None),
        P("dp", None),
        P("mp", "dp"),
        P("mp", "dp"),
        P("dp", "mp"),
    )
    return jax.shard_map(
        shards,
        mesh=mesh,
        in_specs=placed,
        out_specs=(P("dp", "mp"), P("mp", "dp"), P("mp", "dp")),
        check_vma=False,
    )
```

```python
import jax
import jax.numpy as jnp
from jax import lax
from jax.sharding import PartitionSpec as P


SLOTS = 128
LIVE = SLOTS * 5 // 8


def silu_parts(gate_in):
    sigmoid_val = jax.nn.sigmoid(gate_in)
    return (gate_in * sigmoid_val, sigmoid_val * (1.0 + gate_in * (1.0 - sigmoid_val)))


def mp_gather(hidden):
    n_mp = lax.axis_size("mp")
    half = n_mp // 2
    me = lax.axis_index("mp")
    far = lax.ppermute(hidden, "mp", [(i, (i + half) % n_mp) for i in range(n_mp)])
    pair = jnp.stack([hidden, far])
    near = lax.ppermute(pair, "mp", [(i, i ^ 1) for i in range(n_mp)])
    held = jnp.concatenate([pair, near])
    block = jnp.arange(n_mp, dtype=jnp.int32)
    where = jnp.where(((block ^ me) % half) == 0, 0, 1) * 2 + jnp.where((block ^ me) >= half, 1, 0)
    return jnp.take(held, where, axis=0, mode="clip").reshape(n_mp * hidden.shape[0], hidden.shape[1])


def dp_gather_small(block):
    n = lax.axis_size("dp")
    me = lax.axis_index("dp")
    held = block
    step = 1
    while step < n:
        theirs = lax.ppermute(held, "dp", [(i, i ^ step) for i in range(n)])
        low = (me & step) == 0
        held = jnp.where(low, jnp.concatenate([held, theirs]), jnp.concatenate([theirs, held]))
        step *= 2
    return held


def body(sample_grad, advantage, route_rows, route_count, gate_pre, up_pre, down_weight):
    learners = lax.axis_size("dp")
    capacity = SLOTS // learners

    own = route_count[0]
    own_end = jnp.cumsum(own)
    pos = jnp.arange(LIVE, dtype=jnp.int32)
    before = own_end[None, :] <= pos[:, None]
    own_m = jnp.sum(before.astype(jnp.int32), axis=1)
    own_c = pos - jnp.sum(jnp.where(before, own[None, :], 0), axis=1)
    weights = advantage.astype(jnp.float32) * (1.0 / 4096.0)
    scaled_all = (sample_grad.astype(jnp.float32) * weights[:, None]).astype(jnp.bfloat16)
    q_of = own_m * capacity + own_c
    q_pick = (jnp.arange(SLOTS, dtype=jnp.int32)[None, :] == q_of[:, None]).astype(jnp.bfloat16)
    r_pick = (route_rows[0][:SLOTS, None] == jnp.arange(sample_grad.shape[0], dtype=jnp.int32)[None, :])
    pick = jnp.dot(q_pick, r_pick.astype(jnp.bfloat16), preferred_element_type=jnp.float32).astype(jnp.bfloat16)
    scaled = jnp.dot(pick, scaled_all, preferred_element_type=jnp.float32).astype(jnp.bfloat16)
    sent, gate_late, up_late, own_late = lax.optimization_barrier((scaled, gate_pre, up_pre, route_count))
    gate_in = gate_late.astype(jnp.float32)
    up_in = up_late.astype(jnp.float32)
    activated, slopes = silu_parts(gate_in)
    hidden = (activated * up_in).astype(jnp.bfloat16)
    gathered = lax.all_gather(sent, "dp", axis=0, tiled=True)
    hidden_all = mp_gather(hidden)
    counts = dp_gather_small(own_late)

    everything = gathered

    ends = jnp.cumsum(counts, axis=1)
    starts = ends - counts
    done = ends[:, None, :] <= pos[None, :, None]
    m_of = jnp.sum(done.astype(jnp.int32), axis=2)
    c_of = pos[None, :] - jnp.sum(jnp.where(done, counts[:, None, :], 0), axis=2)
    sender = jnp.arange(learners, dtype=jnp.int32)[:, None]
    slot_of = (m_of * SLOTS + sender * capacity + c_of).reshape(-1)
    hidden_live = hidden_all[slot_of]
    everything, hidden_live = lax.optimization_barrier((everything, hidden_live))

    partial_live = lax.dot_general(
        everything, down_weight, (((1,), (1,)), ((), ())), preferred_element_type=jnp.float32
    )

    lane = jnp.arange(capacity, dtype=jnp.int32)
    live = (lane[None, None, :] < counts.T[:, :, None]).reshape(-1)
    first = jnp.arange(learners, dtype=jnp.int32)[None, :] * LIVE + starts.T
    source = jnp.where(live, (first[:, :, None] + lane[None, None, :]).reshape(-1), 0)

    me = lax.axis_index("mp")
    n_mp = lax.axis_size("mp")
    rows_per = hidden.shape[0]

    def partial_block(partial, b):
        return partial[lax.dynamic_slice_in_dim(source, b * rows_per, rows_per)]

    pairs_core = [(i, i ^ 1) for i in range(n_mp)]
    from_core = lax.ppermute(partial_block(partial_live, me ^ 3), "mp", pairs_core)
    to_chip = (partial_block(partial_live, me ^ 2) + from_core).astype(jnp.bfloat16)
    to_chip, partial_late = lax.optimization_barrier((to_chip, partial_live))
    from_chip = lax.ppermute(to_chip, "mp", [(i, i ^ 2) for i in range(n_mp)])
    from_core_own = lax.ppermute(partial_block(partial_late, me ^ 1), "mp", pairs_core)
    own_part = partial_block(partial_late, me)
    grad_down = lax.dot_general(
        hidden_live, everything, (((0,), (0,)), ((), ())), preferred_element_type=jnp.float32
    )
    hidden_grad = (own_part + from_core_own) + from_chip.astype(jnp.float32)
    hidden_grad = jnp.where(lax.dynamic_slice_in_dim(live, me * rows_per, rows_per)[:, None], hidden_grad, 0.0)
    grad_gate = (hidden_grad * up_in * slopes).astype(jnp.bfloat16)
    grad_up = (hidden_grad * activated).astype(jnp.bfloat16)
    return (grad_down, grad_gate, grad_up)


def solution(mesh):
    placed = (
        P("dp", "mp"),
        P("dp"),
        P("dp", None),
        P("dp", None),
        P("mp", "dp"),
        P("mp", "dp"),
        P("dp", "mp"),
    )
    return jax.shard_map(
        body,
        mesh=mesh,
        in_specs=placed,
        out_specs=(P("dp", "mp"), P("mp", "dp"), P("mp", "dp")),
        check_vma=False,
    )
```

```python
import jax
import jax.numpy as jnp
from jax import lax
from jax.sharding import PartitionSpec as P


SLOTS = 128
LIVE = SLOTS * 5 // 8


def silu_parts(gate_in):
    sigmoid_val = jax.nn.sigmoid(gate_in)
    return (gate_in * sigmoid_val, sigmoid_val * (1.0 + gate_in * (1.0 - sigmoid_val)))


def mp_gather(hidden):
    n_mp = lax.axis_size("mp")
    half = n_mp // 2
    me = lax.axis_index("mp")
    far = lax.ppermute(hidden, "mp", [(i, (i + half) % n_mp) for i in range(n_mp)])
    pair = jnp.stack([hidden, far])
    near = lax.ppermute(pair, "mp", [(i, i ^ 1) for i in range(n_mp)])
    held = jnp.concatenate([pair, near])
    block = jnp.arange(n_mp, dtype=jnp.int32)
    where = jnp.where(((block ^ me) % half) == 0, 0, 1) * 2 + jnp.where((block ^ me) >= half, 1, 0)
    return jnp.take(held, where, axis=0, mode="clip").reshape(n_mp * hidden.shape[0], hidden.shape[1])


def dp_gather_small(block):
    n = lax.axis_size("dp")
    me = lax.axis_index("dp")
    held = block
    step = 1
    while step < n:
        theirs = lax.ppermute(held, "dp", [(i, i ^ step) for i in range(n)])
        low = (me & step) == 0
        held = jnp.where(low, jnp.concatenate([held, theirs]), jnp.concatenate([theirs, held]))
        step *= 2
    return held


def body(sample_grad, advantage, route_rows, route_count, gate_pre, up_pre, down_weight):
    learners = lax.axis_size("dp")
    capacity = SLOTS // learners

    own = route_count[0]
    own_end = jnp.cumsum(own)
    pos = jnp.arange(LIVE, dtype=jnp.int32)
    before = own_end[None, :] <= pos[:, None]
    own_m = jnp.sum(before.astype(jnp.int32), axis=1)
    own_c = pos - jnp.sum(jnp.where(before, own[None, :], 0), axis=1)
    weights = advantage.astype(jnp.float32) * (1.0 / 4096.0)
    scaled_all = (sample_grad.astype(jnp.float32) * weights[:, None]).astype(jnp.bfloat16)
    q_of = own_m * capacity + own_c
    q_pick = (jnp.arange(SLOTS, dtype=jnp.int32)[None, :] == q_of[:, None]).astype(jnp.bfloat16)
    r_pick = (route_rows[0][:SLOTS, None] == jnp.arange(sample_grad.shape[0], dtype=jnp.int32)[None, :])
    pick = jnp.dot(q_pick, r_pick.astype(jnp.bfloat16), preferred_element_type=jnp.float32).astype(jnp.bfloat16)
    scaled = jnp.dot(pick, scaled_all, preferred_element_type=jnp.float32).astype(jnp.bfloat16)
    sent, gate_late, up_late, own_late = lax.optimization_barrier((scaled, gate_pre, up_pre, route_count))
    gate_in = gate_late.astype(jnp.float32)
    up_in = up_late.astype(jnp.float32)
    activated, slopes = silu_parts(gate_in)
    hidden = (activated * up_in).astype(jnp.bfloat16)
    gathered = lax.all_gather(sent, "dp", axis=0, tiled=True)
    hidden_all = mp_gather(hidden)
    counts = dp_gather_small(own_late)

    everything = gathered

    ends = jnp.cumsum(counts, axis=1)
    starts = ends - counts
    done = ends[:, None, :] <= pos[None, :, None]
    m_of = jnp.sum(done.astype(jnp.int32), axis=2)
    c_of = pos[None, :] - jnp.sum(jnp.where(done, counts[:, None, :], 0), axis=2)
    sender = jnp.arange(learners, dtype=jnp.int32)[:, None]
    slot_of = (m_of * SLOTS + sender * capacity + c_of).reshape(-1)
    hidden_live = hidden_all[slot_of]
    me = lax.axis_index("mp")
    rows_per = hidden.shape[0]
    lane = jnp.arange(capacity, dtype=jnp.int32)
    live = (lane[None, None, :] < counts.T[:, :, None]).reshape(-1)
    keep = lax.dynamic_slice_in_dim(live, me * rows_per, rows_per)[:, None]
    gate_factor = jnp.where(keep, up_in * slopes, 0.0)
    up_factor = jnp.where(keep, activated, 0.0)
    everything, hidden_live, gate_factor, up_factor = lax.optimization_barrier(
        (everything, hidden_live, gate_factor, up_factor)
    )

    partial_live = lax.dot_general(
        everything, down_weight, (((1,), (1,)), ((), ())), preferred_element_type=jnp.float32
    )

    first = jnp.arange(learners, dtype=jnp.int32)[None, :] * LIVE + starts.T
    source = jnp.where(live, (first[:, :, None] + lane[None, None, :]).reshape(-1), 0)

    n_mp = lax.axis_size("mp")

    def partial_block(partial, b):
        return partial[lax.dynamic_slice_in_dim(source, b * rows_per, rows_per)]

    pairs_core = [(i, i ^ 1) for i in range(n_mp)]
    from_core = lax.ppermute(partial_block(partial_live, me ^ 3), "mp", pairs_core)
    to_chip = (partial_block(partial_live, me ^ 2) + from_core).astype(jnp.bfloat16)
    to_chip, partial_late = lax.optimization_barrier((to_chip, partial_live))
    from_chip = lax.ppermute(to_chip, "mp", [(i, i ^ 2) for i in range(n_mp)])
    from_core_own = lax.ppermute(partial_block(partial_late, me ^ 1), "mp", pairs_core)
    own_part = partial_block(partial_late, me)
    grad_down = lax.dot_general(
        hidden_live, everything, (((0,), (0,)), ((), ())), preferred_element_type=jnp.float32
    )
    hidden_grad = (own_part + from_core_own) + from_chip.astype(jnp.float32)
    grad_gate = (hidden_grad * gate_factor).astype(jnp.bfloat16)
    grad_up = (hidden_grad * up_factor).astype(jnp.bfloat16)
    return (grad_down, grad_gate, grad_up)


def solution(mesh):
    placed = (
        P("dp", "mp"),
        P("dp"),
        P("dp", None),
        P("dp", None),
        P("mp", "dp"),
        P("mp", "dp"),
        P("dp", "mp"),
    )
    return jax.shard_map(
        body,
        mesh=mesh,
        in_specs=placed,
        out_specs=(P("dp", "mp"), P("mp", "dp"), P("mp", "dp")),
        check_vma=False,
    )
```

```python
import jax
import jax.numpy as jnp
from jax import lax
from jax.sharding import PartitionSpec as P


SLOTS = 128
LIVE = SLOTS * 5 // 8


def silu_parts(gate_in):
    sigmoid_val = jax.nn.sigmoid(gate_in)
    return (gate_in * sigmoid_val, sigmoid_val * (1.0 + gate_in * (1.0 - sigmoid_val)))


def mp_gather(hidden):
    n_mp = lax.axis_size("mp")
    half = n_mp // 2
    me = lax.axis_index("mp")
    far = lax.ppermute(hidden, "mp", [(i, (i + half) % n_mp) for i in range(n_mp)])
    pair = jnp.stack([hidden, far])
    near = lax.ppermute(pair, "mp", [(i, i ^ 1) for i in range(n_mp)])
    held = jnp.concatenate([pair, near])
    block = jnp.arange(n_mp, dtype=jnp.int32)
    where = jnp.where(((block ^ me) % half) == 0, 0, 1) * 2 + jnp.where((block ^ me) >= half, 1, 0)
    return jnp.take(held, where, axis=0, mode="clip").reshape(n_mp * hidden.shape[0], hidden.shape[1])


def dp_gather_small(block):
    n = lax.axis_size("dp")
    me = lax.axis_index("dp")
    held = block
    step = 1
    while step < n:
        theirs = lax.ppermute(held, "dp", [(i, i ^ step) for i in range(n)])
        low = (me & step) == 0
        held = jnp.where(low, jnp.concatenate([held, theirs]), jnp.concatenate([theirs, held]))
        step *= 2
    return held


def body(sample_grad, advantage, route_rows, route_count, gate_pre, up_pre, down_weight):
    learners = lax.axis_size("dp")
    capacity = SLOTS // learners

    own = route_count[0]
    own_end = jnp.cumsum(own)
    pos = jnp.arange(LIVE, dtype=jnp.int32)
    before = own_end[None, :] <= pos[:, None]
    own_m = jnp.sum(before.astype(jnp.int32), axis=1)
    own_c = pos - jnp.sum(jnp.where(before, own[None, :], 0), axis=1)
    weights = advantage.astype(jnp.float32) * (1.0 / 4096.0)
    scaled_all = (sample_grad.astype(jnp.float32) * weights[:, None]).astype(jnp.bfloat16)
    q_of = own_m * capacity + own_c
    q_pick = (jnp.arange(SLOTS, dtype=jnp.int32)[None, :] == q_of[:, None]).astype(jnp.bfloat16)
    r_pick = (route_rows[0][:SLOTS, None] == jnp.arange(sample_grad.shape[0], dtype=jnp.int32)[None, :])
    pick = jnp.dot(q_pick, r_pick.astype(jnp.bfloat16), preferred_element_type=jnp.float32).astype(jnp.bfloat16)
    scaled = jnp.dot(pick, scaled_all, preferred_element_type=jnp.float32).astype(jnp.bfloat16)
    sent, gate_late, up_late, own_late = lax.optimization_barrier((scaled, gate_pre, up_pre, route_count))
    gate_in = gate_late.astype(jnp.float32)
    up_in = up_late.astype(jnp.float32)
    activated, slopes = silu_parts(gate_in)
    hidden = (activated * up_in).astype(jnp.bfloat16)
    gathered = lax.all_gather(sent, "dp", axis=0, tiled=True)
    hidden_all = mp_gather(hidden)
    counts = dp_gather_small(own_late)

    everything = gathered

    ends = jnp.cumsum(counts, axis=1)
    starts = ends - counts
    done = ends[:, None, :] <= pos[None, :, None]
    m_of = jnp.sum(done.astype(jnp.int32), axis=2)
    c_of = pos[None, :] - jnp.sum(jnp.where(done, counts[:, None, :], 0), axis=2)
    sender = jnp.arange(learners, dtype=jnp.int32)[:, None]
    slot_of = (m_of * SLOTS + sender * capacity + c_of).reshape(-1)
    hidden_live = hidden_all.at[slot_of].get(mode="promise_in_bounds")
    everything, hidden_live = lax.optimization_barrier((everything, hidden_live))

    partial_live = lax.dot_general(
        everything, down_weight, (((1,), (1,)), ((), ())), preferred_element_type=jnp.float32
    )

    lane = jnp.arange(capacity, dtype=jnp.int32)
    live = (lane[None, None, :] < counts.T[:, :, None]).reshape(-1)
    first = jnp.arange(learners, dtype=jnp.int32)[None, :] * LIVE + starts.T
    source = jnp.where(live, (first[:, :, None] + lane[None, None, :]).reshape(-1), 0)

    me = lax.axis_index("mp")
    n_mp = lax.axis_size("mp")
    rows_per = hidden.shape[0]

    def partial_block(partial, b):
        rows = lax.dynamic_slice_in_dim(source, b * rows_per, rows_per)
        return partial.at[rows].get(mode="promise_in_bounds")

    pairs_core = [(i, i ^ 1) for i in range(n_mp)]
    from_core = lax.ppermute(partial_block(partial_live, me ^ 3), "mp", pairs_core)
    to_chip = (partial_block(partial_live, me ^ 2) + from_core).astype(jnp.bfloat16)
    to_chip, partial_late = lax.optimization_barrier((to_chip, partial_live))
    from_chip = lax.ppermute(to_chip, "mp", [(i, i ^ 2) for i in range(n_mp)])
    from_core_own = lax.ppermute(partial_block(partial_late, me ^ 1), "mp", pairs_core)
    own_part = partial_block(partial_late, me)
    grad_down = lax.dot_general(
        hidden_live, everything, (((0,), (0,)), ((), ())), preferred_element_type=jnp.float32
    )
    hidden_grad = (own_part + from_core_own) + from_chip.astype(jnp.float32)
    hidden_grad = jnp.where(lax.dynamic_slice_in_dim(live, me * rows_per, rows_per)[:, None], hidden_grad, 0.0)
    grad_gate = (hidden_grad * up_in * slopes).astype(jnp.bfloat16)
    grad_up = (hidden_grad * activated).astype(jnp.bfloat16)
    return (grad_down, grad_gate, grad_up)


def solution(mesh):
    placed = (
        P("dp", "mp"),
        P("dp"),
        P("dp", None),
        P("dp", None),
        P("mp", "dp"),
        P("mp", "dp"),
        P("dp", "mp"),
    )
    return jax.shard_map(
        body,
        mesh=mesh,
        in_specs=placed,
        out_specs=(P("dp", "mp"), P("mp", "dp"), P("mp", "dp")),
        check_vma=False,
    )
```

```python
import jax
import jax.numpy as jnp
from jax import lax
from jax.sharding import PartitionSpec as P


SLOTS = 128
LIVE = SLOTS * 5 // 8


def silu_parts(gate_in):
    sigmoid_val = jax.nn.sigmoid(gate_in)
    return (gate_in * sigmoid_val, sigmoid_val * (1.0 + gate_in * (1.0 - sigmoid_val)))


def mp_gather(hidden):
    n_mp = lax.axis_size("mp")
    half = n_mp // 2
    me = lax.axis_index("mp")
    far = lax.ppermute(hidden, "mp", [(i, (i + half) % n_mp) for i in range(n_mp)])
    pair = jnp.stack([hidden, far])
    near = lax.ppermute(pair, "mp", [(i, i ^ 1) for i in range(n_mp)])
    held = jnp.concatenate([pair, near])
    block = jnp.arange(n_mp, dtype=jnp.int32)
    where = jnp.where(((block ^ me) % half) == 0, 0, 1) * 2 + jnp.where((block ^ me) >= half, 1, 0)
    return jnp.take(held, where, axis=0, mode="clip").reshape(n_mp * hidden.shape[0], hidden.shape[1])


def dp_gather_small(block):
    n = lax.axis_size("dp")
    me = lax.axis_index("dp")
    held = block
    step = 1
    while step < n:
        theirs = lax.ppermute(held, "dp", [(i, i ^ step) for i in range(n)])
        low = (me & step) == 0
        held = jnp.where(low, jnp.concatenate([held, theirs]), jnp.concatenate([theirs, held]))
        step *= 2
    return held


def body(sample_grad, advantage, route_rows, route_count, gate_pre, up_pre, down_weight):
    learners = lax.axis_size("dp")
    capacity = SLOTS // learners

    own = route_count[0]
    own_end = jnp.cumsum(own)
    pos = jnp.arange(LIVE, dtype=jnp.int32)
    before = own_end[None, :] <= pos[:, None]
    own_m = jnp.sum(before.astype(jnp.int32), axis=1)
    own_c = pos - jnp.sum(jnp.where(before, own[None, :], 0), axis=1)
    weights = advantage.astype(jnp.float32) * (1.0 / 4096.0)
    scaled_all = (sample_grad.astype(jnp.float32) * weights[:, None]).astype(jnp.bfloat16)
    q_of = own_m * capacity + own_c
    q_pick = (jnp.arange(SLOTS, dtype=jnp.int32)[None, :] == q_of[:, None]).astype(jnp.bfloat16)
    r_pick = (route_rows[0][:SLOTS, None] == jnp.arange(sample_grad.shape[0], dtype=jnp.int32)[None, :])
    pick = jnp.dot(q_pick, r_pick.astype(jnp.bfloat16), preferred_element_type=jnp.float32).astype(jnp.bfloat16)
    scaled = jnp.dot(pick, scaled_all, preferred_element_type=jnp.float32).astype(jnp.bfloat16)
    sent, gate_late, up_late, own_late = lax.optimization_barrier((scaled, gate_pre, up_pre, route_count))
    gate_in = gate_late.astype(jnp.float32)
    up_in = up_late.astype(jnp.float32)
    activated, slopes = silu_parts(gate_in)
    hidden = (activated * up_in).astype(jnp.bfloat16)
    gathered = lax.all_gather(sent, "dp", axis=0, tiled=True)
    hidden_all = mp_gather(hidden)
    counts = dp_gather_small(own_late)

    everything = gathered

    ends = jnp.cumsum(counts, axis=1)
    starts = ends - counts
    done = ends[:, None, :] <= pos[None, :, None]
    m_of = jnp.sum(done.astype(jnp.int32), axis=2)
    c_of = pos[None, :] - jnp.sum(jnp.where(done, counts[:, None, :], 0), axis=2)
    sender = jnp.arange(learners, dtype=jnp.int32)[:, None]
    slot_of = (m_of * SLOTS + sender * capacity + c_of).reshape(-1)
    hidden_live = hidden_all[slot_of]
    everything, hidden_live = lax.optimization_barrier((everything, hidden_live))

    partial_live = lax.dot_general(
        everything, down_weight, (((1,), (1,)), ((), ())), preferred_element_type=jnp.float32
    )

    lane = jnp.arange(capacity, dtype=jnp.int32)
    live = (lane[None, None, :] < counts.T[:, :, None]).reshape(-1)
    first = jnp.arange(learners, dtype=jnp.int32)[None, :] * LIVE + starts.T
    source = jnp.where(live, (first[:, :, None] + lane[None, None, :]).reshape(-1), 0)

    me = lax.axis_index("mp")
    n_mp = lax.axis_size("mp")
    rows_per = hidden.shape[0]

    def partial_block(partial, b):
        return partial[lax.dynamic_slice_in_dim(source, b * rows_per, rows_per)]

    pairs_core = [(i, i ^ 1) for i in range(n_mp)]
    from_core = lax.ppermute(partial_block(partial_live, me ^ 3), "mp", pairs_core)
    to_chip = (partial_block(partial_live, me ^ 2) + from_core).astype(jnp.bfloat16)
    to_chip, partial_late = lax.optimization_barrier((to_chip, partial_live))
    from_chip = lax.ppermute(to_chip, "mp", [(i, i ^ 2) for i in range(n_mp)])
    rows = jnp.concatenate(
        [lax.dynamic_slice_in_dim(source, b * rows_per, rows_per) for b in (me ^ 1, me)]
    )
    late_blocks = partial_late[rows]
    from_core_own = lax.ppermute(late_blocks[:rows_per], "mp", pairs_core)
    own_part = late_blocks[rows_per:]
    grad_down = lax.dot_general(
        hidden_live, everything, (((0,), (0,)), ((), ())), preferred_element_type=jnp.float32
    )
    hidden_grad = (own_part + from_core_own) + from_chip.astype(jnp.float32)
    hidden_grad = jnp.where(lax.dynamic_slice_in_dim(live, me * rows_per, rows_per)[:, None], hidden_grad, 0.0)
    grad_gate = (hidden_grad * up_in * slopes).astype(jnp.bfloat16)
    grad_up = (hidden_grad * activated).astype(jnp.bfloat16)
    return (grad_down, grad_gate, grad_up)


def solution(mesh):
    placed = (
        P("dp", "mp"),
        P("dp"),
        P("dp", None),
        P("dp", None),
        P("mp", "dp"),
        P("mp", "dp"),
        P("dp", "mp"),
    )
    return jax.shard_map(
        body,
        mesh=mesh,
        in_specs=placed,
        out_specs=(P("dp", "mp"), P("mp", "dp"), P("mp", "dp")),
        check_vma=False,
    )
```

```python
import jax
import jax.numpy as jnp
from jax import lax
from jax.sharding import PartitionSpec as P


SLOTS = 128
LIVE = SLOTS * 5 // 8


def silu_parts(gate_in):
    sigmoid_val = jax.nn.sigmoid(gate_in)
    return (gate_in * sigmoid_val, sigmoid_val * (1.0 + gate_in * (1.0 - sigmoid_val)))


def mp_gather(hidden):
    n_mp = lax.axis_size("mp")
    half = n_mp // 2
    me = lax.axis_index("mp")
    far = lax.ppermute(hidden, "mp", [(i, (i + half) % n_mp) for i in range(n_mp)])
    pair = jnp.stack([hidden, far])
    near = lax.ppermute(pair, "mp", [(i, i ^ 1) for i in range(n_mp)])
    held = jnp.concatenate([pair, near])
    block = jnp.arange(n_mp, dtype=jnp.int32)
    where = jnp.where(((block ^ me) % half) == 0, 0, 1) * 2 + jnp.where((block ^ me) >= half, 1, 0)
    return jnp.take(held, where, axis=0, mode="clip").reshape(n_mp * hidden.shape[0], hidden.shape[1])


def dp_gather_small(block):
    n = lax.axis_size("dp")
    me = lax.axis_index("dp")
    held = block
    step = 1
    while step < n:
        theirs = lax.ppermute(held, "dp", [(i, i ^ step) for i in range(n)])
        low = (me & step) == 0
        held = jnp.where(low, jnp.concatenate([held, theirs]), jnp.concatenate([theirs, held]))
        step *= 2
    return held


def body(sample_grad, advantage, route_rows, route_count, gate_pre, up_pre, down_weight):
    learners = lax.axis_size("dp")
    capacity = SLOTS // learners

    own = route_count[0]
    own_end = jnp.cumsum(own)
    pos = jnp.arange(LIVE, dtype=jnp.int32)
    before = own_end[None, :] <= pos[:, None]
    own_m = jnp.sum(before.astype(jnp.int32), axis=1)
    own_c = pos - jnp.sum(jnp.where(before, own[None, :], 0), axis=1)
    weights = advantage.astype(jnp.float32) * (1.0 / 4096.0)
    scaled_all = (sample_grad.astype(jnp.float32) * weights[:, None]).astype(jnp.bfloat16)
    q_of = own_m * capacity + own_c
    q_pick = (jnp.arange(SLOTS, dtype=jnp.int32)[None, :] == q_of[:, None]).astype(jnp.bfloat16)
    r_pick = (route_rows[0][:SLOTS, None] == jnp.arange(sample_grad.shape[0], dtype=jnp.int32)[None, :])
    pick = jnp.dot(q_pick, r_pick.astype(jnp.bfloat16), preferred_element_type=jnp.float32).astype(jnp.bfloat16)
    scaled = jnp.dot(pick, scaled_all, preferred_element_type=jnp.float32).astype(jnp.bfloat16)
    sent, gate_late, up_late, own_late = lax.optimization_barrier((scaled, gate_pre, up_pre, route_count))
    gate_in = gate_late.astype(jnp.float32)
    up_in = up_late.astype(jnp.float32)
    activated, slopes = silu_parts(gate_in)
    hidden = (activated * up_in).astype(jnp.bfloat16)
    gathered = lax.all_gather(sent, "dp", axis=0, tiled=True)
    hidden_all = mp_gather(hidden)
    counts = dp_gather_small(own_late)

    everything = gathered

    ends = jnp.cumsum(counts, axis=1)
    starts = ends - counts
    done = ends[:, None, :] <= pos[None, :, None]
    m_of = jnp.sum(done.astype(jnp.int32), axis=2)
    c_of = pos[None, :] - jnp.sum(jnp.where(done, counts[:, None, :], 0), axis=2)
    sender = jnp.arange(learners, dtype=jnp.int32)[:, None]
    slot_of = (m_of * SLOTS + sender * capacity + c_of).reshape(-1)
    hidden_live = hidden_all[slot_of]
    everything, hidden_live = lax.optimization_barrier((everything, hidden_live))

    partial_live = lax.dot_general(
        everything, down_weight, (((1,), (1,)), ((), ())), preferred_element_type=jnp.float32
    )

    lane = jnp.arange(capacity, dtype=jnp.int32)
    live = (lane[None, None, :] < counts.T[:, :, None]).reshape(-1)
    first = jnp.arange(learners, dtype=jnp.int32)[None, :] * LIVE + starts.T
    source = jnp.where(live, (first[:, :, None] + lane[None, None, :]).reshape(-1), 0)

    me = lax.axis_index("mp")
    n_mp = lax.axis_size("mp")
    rows_per = hidden.shape[0]

    def partial_block(partial, b):
        return partial[lax.dynamic_slice_in_dim(source, b * rows_per, rows_per)]

    pairs_core = [(i, i ^ 1) for i in range(n_mp)]
    from_core = lax.ppermute(partial_block(partial_live, me ^ 3), "mp", pairs_core)
    to_chip = (partial_block(partial_live, me ^ 2) + from_core).astype(jnp.bfloat16)
    to_chip, partial_late = lax.optimization_barrier((to_chip, partial_live))
    from_chip = lax.ppermute(to_chip, "mp", [(i, i ^ 2) for i in range(n_mp)])
    rows = jnp.stack(
        [lax.dynamic_slice_in_dim(source, b * rows_per, rows_per) for b in (me ^ 1, me)]
    )
    late_blocks = partial_late[rows]
    from_core_own = lax.ppermute(late_blocks[0], "mp", pairs_core)
    own_part = late_blocks[1]
    grad_down = lax.dot_general(
        hidden_live, everything, (((0,), (0,)), ((), ())), preferred_element_type=jnp.float32
    )
    hidden_grad = (own_part + from_core_own) + from_chip.astype(jnp.float32)
    hidden_grad = jnp.where(lax.dynamic_slice_in_dim(live, me * rows_per, rows_per)[:, None], hidden_grad, 0.0)
    grad_gate = (hidden_grad * up_in * slopes).astype(jnp.bfloat16)
    grad_up = (hidden_grad * activated).astype(jnp.bfloat16)
    return (grad_down, grad_gate, grad_up)


def solution(mesh):
    placed = (
        P("dp", "mp"),
        P("dp"),
        P("dp", None),
        P("dp", None),
        P("mp", "dp"),
        P("mp", "dp"),
        P("dp", "mp"),
    )
    return jax.shard_map(
        body,
        mesh=mesh,
        in_specs=placed,
        out_specs=(P("dp", "mp"), P("mp", "dp"), P("mp", "dp")),
        check_vma=False,
    )
```
